256 devices in a mesh: row: 16 (over z_lo, y), col: 8 (over x, core), layer: 2 (over z_hi).
Axes of the slice: x: 4, y: 4, z: 8 (z_hi: 2, z_lo: 4; z = z_hi * 4 + z_lo), core: 2. Of those that a mesh axis runs over, the one named last changes fastest.
Arguments:
- density: float32 [2, 8192, 2048], P('layer', 'row', 'col'), may hold values from -6 to 6
- dens_mask: int32 [2, 128, 32], P('layer', 'row', 'col'), may hold values from 0 to 1, as said below
- hamiltonian: float32 [2, 2048, 16384], P('layer', 'row', 'col'), may hold values from -0.375 to 0.375
- ham_mask: int32 [2, 32, 256], P('layer', None, 'col'), may hold values from 0 to 1, as said below
- filter_mask: int32 [128, 256], P('row', 'col'), may hold values from 0 to 1, as said below
Outputs:
- product: float32 [8192, 16384], P('row', ('col', 'layer'))
The draws below stay inside these ranges and needn't reach their ends.
Inputs may be any that keep to these rules, and one draw needn't show every extreme that they name: `dens_mask`: 1 where a density block is nonzero, else 0. `ham_mask`: 1 where a Hamiltonian block is nonzero, else 0. `filter_mask`: 1 where a result block is kept, else 0.
All inputs are finite; a program needn't handle non-finite values.
Results may differ from the reference program's by a relative error of at most 0.0001.
Values sent between devices are 32-bit elements; how exact they have to be, the bound alone decides.
No kernel may reach another device: no remote copies, remote signals or barrier semaphores. Data moves between devices by JAX's collectives and lax.ppermute only.
A program may use at most 128 MiB of HBM per device.

```python
import jax
import jax.numpy as jnp
from jax import lax

BLOCK = 64
MB_ALL = 128
KB_HALF = 32
NB_ALL = 256
N_LAYER = 2


def band_mask(key, row_pos, col_pos):
    key_shift, key_width, key_extra = jax.random.split(key, 3)
    offset = jax.random.randint(key_shift, (), 0, 1000, dtype=jnp.int32)
    widths = jax.random.randint(key_width, row_pos.shape, 150, 450, dtype=jnp.int32)
    apart = jnp.abs(row_pos[:, None] - (col_pos[None, :] + offset) % 1000)
    cyclic = jnp.minimum(apart, 1000 - apart)
    scatter = jax.random.randint(key_extra, cyclic.shape, 0, 100, dtype=jnp.int32) < 10
    return ((cyclic < widths[:, None]) | scatter).astype(jnp.int32)


def draw_dens_mask(key, part):
    inner_total = N_LAYER * KB_HALF
    row_pos = jnp.arange(MB_ALL, dtype=jnp.int32) * 1000 // MB_ALL
    inner_pos = jnp.arange(inner_total, dtype=jnp.int32) * 1000 // inner_total
    whole = band_mask(jax.random.fold_in(key, 11), row_pos, inner_pos)
    return jnp.transpose(whole.reshape(MB_ALL, N_LAYER, KB_HALF), (1, 0, 2))


def draw_ham_mask(key, part):
    inner_total = N_LAYER * KB_HALF
    inner_pos = jnp.arange(inner_total, dtype=jnp.int32) * 1000 // inner_total
    col_pos = jnp.arange(NB_ALL, dtype=jnp.int32) * 1000 // NB_ALL
    whole = band_mask(jax.random.fold_in(key, 23), inner_pos, col_pos)
    return whole.reshape(N_LAYER, KB_HALF, NB_ALL)


def draw_filter_mask(key, part):
    row_pos = jnp.arange(MB_ALL, dtype=jnp.int32) * 1000 // MB_ALL
    col_pos = jnp.arange(NB_ALL, dtype=jnp.int32) * 1000 // NB_ALL
    return band_mask(jax.random.fold_in(key, 37), row_pos, col_pos)


def steps_of(rng, extent, pieces, least, top_value):
    def one(dim, blocks):
        steps = jax.random.uniform(jax.random.fold_in(jax.random.fold_in(rng, 6), dim), (blocks,), jnp.float32, least / len(pieces), top_value / len(pieces))
        return jnp.repeat(jnp.exp(steps), extent[dim] // blocks).reshape((-1,) + (1,) * (len(extent) - dim - 1))

    loudness = one(*pieces[0])
    for cut in pieces[1:]:
        loudness = loudness * one(*cut)
    return loudness


def scatter_about(stream_key, dims, scale, most, cuts=(), held_as=jnp.bfloat16):
    entries = jax.random.normal(stream_key, dims, jnp.float32) * scale
    if len(cuts) > 0:
        entries = steps_of(stream_key, dims, cuts, -0.22, 0.18) * entries
    return jnp.clip(entries, min=-most, max=most).astype(held_as)


def setup_inputs(seed: int = 0) -> dict:
    key_list = jax.random.split(jax.random.key(seed), 6)
    return {
        "density": scatter_about(key_list[0], (N_LAYER, MB_ALL * BLOCK, KB_HALF * BLOCK), 1.0, 6.0, ((0, 2), (1, 16), (2, 8)), jnp.float32),
        "dens_mask": draw_dens_mask(jax.random.fold_in(key_list[5], 71), 0),
        "hamiltonian": scatter_about(key_list[2], (N_LAYER, KB_HALF * BLOCK, NB_ALL * BLOCK), (BLOCK * 4) ** -0.5, 0.375, ((0, 2), (1, 16), (2, 8)), jnp.float32),
        "ham_mask": draw_ham_mask(jax.random.fold_in(key_list[5], 71), 0),
        "filter_mask": draw_filter_mask(jax.random.fold_in(key_list[5], 71), 0),
    }


def expand(block_mask):
    widened = jnp.repeat(block_mask.astype(jnp.float32), BLOCK, axis=-2)
    return jnp.repeat(widened, BLOCK, axis=-1)


def reference(density, dens_mask, hamiltonian, ham_mask, filter_mask):
    dens_eff = density * expand(dens_mask)
    ham_eff = hamiltonian * expand(ham_mask)
    total = jnp.dot(dens_eff[0], ham_eff[0], precision=lax.Precision.HIGHEST, preferred_element_type=jnp.float32)
    for group_pos in range(1, N_LAYER):
        total = total + jnp.dot(dens_eff[group_pos], ham_eff[group_pos], precision=lax.Precision.HIGHEST, preferred_element_type=jnp.float32)
    return total * expand(filter_mask)
```

```python
import jax
import jax.numpy as jnp
from jax import lax
from jax.sharding import PartitionSpec as P

BLOCK = 64
N_CHUNKS = 2


def expand(block_mask):
    widened = jnp.repeat(block_mask.astype(jnp.float32), BLOCK, axis=-2)
    return jnp.repeat(widened, BLOCK, axis=-1)


def shards(density, dens_mask, hamiltonian, ham_mask, filter_mask):
    layer = lax.axis_index("layer")
    n_layer = lax.axis_size("layer")
    dens_vals = (density * expand(dens_mask))[0]
    ham_count = hamiltonian.shape[1]
    picked = lax.dynamic_slice_in_dim(
        ham_mask[0], lax.axis_index("row") * (ham_count // BLOCK), ham_count // BLOCK, axis=0
    )
    ham_vals = hamiltonian[0] * expand(picked)
    cols = ham_vals.shape[1]
    half = cols // n_layer
    width = half // N_CHUNKS
    kept = lax.dynamic_slice_in_dim(expand(filter_mask), layer * half, half, axis=1)

    dens_row = lax.all_gather(dens_vals, "col", axis=1, tiled=True)
    send_half = lax.dynamic_slice_in_dim(ham_vals, (1 - layer) * half, half, axis=1)
    keep_half = lax.dynamic_slice_in_dim(ham_vals, layer * half, half, axis=1)

    def panel(ham_half, j):
        ham_panel = lax.all_gather(ham_half[:, j * width:(j + 1) * width], "row", axis=0, tiled=True)
        return jnp.dot(
            dens_row,
            ham_panel,
            precision=lax.Precision.HIGHEST,
            preferred_element_type=jnp.float32,
        )

    perm = [(0, 1), (1, 0)]
    received = [lax.ppermute(panel(send_half, j), "layer", perm) for j in range(N_CHUNKS)]
    own = [panel(keep_half, j) for j in range(N_CHUNKS)]
    total = jnp.concatenate([a + b for a, b in zip(own, received)], axis=1)
    return total * kept


def solution(mesh):
    return jax.shard_map(
        shards,
        mesh=mesh,
        in_specs=(
            P("layer", "row", "col"),
            P("layer", "row", "col"),
            P("layer", "row", "col"),
            P("layer", None, "col"),
            P("row", "col"),
        ),
        out_specs=P("row", ("col", "layer")),
        check_vma=False,
    )
```

```python
import jax
import jax.numpy as jnp
from jax import lax
from jax.sharding import PartitionSpec as P

BLOCK = 64


def expand(block_mask):
    widened = jnp.repeat(block_mask.astype(jnp.float32), BLOCK, axis=-2)
    return jnp.repeat(widened, BLOCK, axis=-1)


def gather_cols(block, axis_name, n):
    parts = [block]
    for shift in range(1, n):
        parts.append(lax.ppermute(block, axis_name, [((i + shift) % n, i) for i in range(n)]))
    twice = jnp.concatenate(parts + parts, axis=1)
    start = (n - lax.axis_index(axis_name)) * block.shape[1]
    return lax.dynamic_slice_in_dim(twice, start, n * block.shape[1], axis=1)


def product_dot(a, b):
    return jnp.dot(a, b, precision=lax.Precision.HIGHEST, preferred_element_type=jnp.float32)


def shards(density, dens_mask, hamiltonian, ham_mask, filter_mask, n_col):
    layer = lax.axis_index("layer")
    dens_vals = (density * expand(dens_mask))[0]
    ham_count = hamiltonian.shape[1]
    picked = lax.dynamic_slice_in_dim(
        ham_mask[0], lax.axis_index("row") * (ham_count // BLOCK), ham_count // BLOCK, axis=0
    )
    ham_vals = hamiltonian[0] * expand(picked)
    half = ham_vals.shape[1] // 2
    kept = lax.dynamic_slice_in_dim(expand(filter_mask), layer * half, half, axis=1)

    send_half = lax.dynamic_slice_in_dim(ham_vals, (1 - layer) * half, half, axis=1)
    keep_half = lax.dynamic_slice_in_dim(ham_vals, layer * half, half, axis=1)
    ham_send = lax.all_gather(send_half, "row", axis=0, tiled=True)
    dens_row = gather_cols(dens_vals, "col", n_col)
    received = lax.ppermute(product_dot(dens_row, ham_send), "layer", [(0, 1), (1, 0)])
    ham_keep = lax.all_gather(keep_half, "row", axis=0, tiled=True)
    own = product_dot(dens_row, ham_keep)
    return (own + received) * kept


def solution(mesh):
    n_col = mesh.shape["col"]
    return jax.shard_map(
        lambda *args: shards(*args, n_col),
        mesh=mesh,
        in_specs=(
            P("layer", "row", "col"),
            P("layer", "row", "col"),
            P("layer", "row", "col"),
            P("layer", None, "col"),
            P("row", "col"),
        ),
        out_specs=P("row", ("col", "layer")),
        check_vma=False,
    )
```

```python
import jax
import jax.numpy as jnp
from jax import lax
from jax.sharding import PartitionSpec as P

BLOCK = 64


def expand(block_mask):
    widened = jnp.repeat(block_mask.astype(jnp.float32), BLOCK, axis=-2)
    return jnp.repeat(widened, BLOCK, axis=-1)


def gather_cols(block, axis_name, n):
    parts = [block]
    for shift in range(1, n):
        parts.append(lax.ppermute(block, axis_name, [((i + shift) % n, i) for i in range(n)]))
    twice = jnp.concatenate(parts + parts, axis=1)
    start = (n - lax.axis_index(axis_name)) * block.shape[1]
    return lax.dynamic_slice_in_dim(twice, start, n * block.shape[1], axis=1)


def product_dot(a, b):
    return jnp.dot(a, b, precision=lax.Precision.HIGH, preferred_element_type=jnp.float32)


def shards(density, dens_mask, hamiltonian, ham_mask, filter_mask, n_col):
    layer = lax.axis_index("layer")
    dens_vals = (density * expand(dens_mask))[0]
    ham_count = hamiltonian.shape[1]
    picked = lax.dynamic_slice_in_dim(
        ham_mask[0], lax.axis_index("row") * (ham_count // BLOCK), ham_count // BLOCK, axis=0
    )
    ham_vals = hamiltonian[0] * expand(picked)
    half = ham_vals.shape[1] // 2
    kept = lax.dynamic_slice_in_dim(expand(filter_mask), layer * half, half, axis=1)

    send_half = lax.dynamic_slice_in_dim(ham_vals, (1 - layer) * half, half, axis=1)
    keep_half = lax.dynamic_slice_in_dim(ham_vals, layer * half, half, axis=1)
    ham_send = lax.all_gather(send_half, "row", axis=0, tiled=True)
    dens_row = gather_cols(dens_vals, "col", n_col)
    received = lax.ppermute(product_dot(dens_row, ham_send), "layer", [(0, 1), (1, 0)])
    ham_keep = lax.all_gather(keep_half, "row", axis=0, tiled=True)
    own = product_dot(dens_row, ham_keep)
    return (own + received) * kept


def solution(mesh):
    n_col = mesh.shape["col"]
    return jax.shard_map(
        lambda *args: shards(*args, n_col),
        mesh=mesh,
        in_specs=(
            P("layer", "row", "col"),
            P("layer", "row", "col"),
            P("layer", "row", "col"),
            P("layer", None, "col"),
            P("row", "col"),
        ),
        out_specs=P("row", ("col", "layer")),
        check_vma=False,
    )
```

```python
import jax
import jax.numpy as jnp
from jax import lax
from jax.sharding import Mesh
from jax.sharding import PartitionSpec as P

BLOCK = 64
AXES = ("zl", "yh", "yl", "x", "core", "layer")
ROW = ("zl", "yh", "yl")
COL = ("x", "core")


def expand(block_mask):
    widened = jnp.repeat(block_mask.astype(jnp.float32), BLOCK, axis=-2)
    return jnp.repeat(widened, BLOCK, axis=-1)


def product_dot(a, b):
    return jnp.dot(a, b, precision=lax.Precision.HIGH, preferred_element_type=jnp.float32)


def gather_cols(block, index, n):
    parts = [block]
    for shift in range(1, n):
        parts.append(lax.ppermute(block, COL, [((i + shift) % n, i) for i in range(n)]))
    twice = jnp.concatenate(parts + parts, axis=1)
    return lax.dynamic_slice_in_dim(twice, (n - index) * block.shape[1], n * block.shape[1], axis=1)


def shards(density, dens_mask, hamiltonian, ham_mask, filter_mask, n_col):
    yl = lax.axis_index("yl")
    core = lax.axis_index("core")
    layer = lax.axis_index("layer")
    row = (lax.axis_index("zl") * 2 + lax.axis_index("yh")) * 2 + yl
    col = lax.axis_index("x") * 2 + core

    dens_vals = (density * expand(dens_mask))[0]
    ham_count = hamiltonian.shape[1]
    picked = lax.dynamic_slice_in_dim(ham_mask[0], row * (ham_count // BLOCK), ham_count // BLOCK, axis=0)
    ham_vals = hamiltonian[0] * expand(picked)
    half = ham_vals.shape[1] // 2
    kept = lax.dynamic_slice_in_dim(expand(filter_mask), layer * half, half, axis=1)

    pieces = {}
    for h in (0, 1):
        part = ham_vals[:, h * half:(h + 1) * half]
        for j in (0, 1):
            pieces[h, j] = lax.ppermute(part, ("yl", "core"), [(j * 2 + c, c * 2 + h) for c in (0, 1)])
    contrib = jnp.where(
        core == 0,
        jnp.concatenate([pieces[0, 0], pieces[0, 1]], axis=0),
        jnp.concatenate([pieces[1, 0], pieces[1, 1]], axis=0),
    )
    ham_own = lax.all_gather(contrib, ("zl", "yh"), axis=0, tiled=True)
    ham_other = lax.ppermute(ham_own, "core", [(0, 1), (1, 0)])

    dens_own = gather_cols(dens_vals, col, n_col)
    dens_nbr = lax.ppermute(dens_own, ("yl", "core"), [(0, 2), (3, 1)])
    dens_rows = jnp.where(core == yl, dens_own, dens_nbr)

    part_own = product_dot(dens_rows, ham_own)
    part_other = product_dot(dens_rows, ham_other)

    def route(value, target_layer):
        perm = []
        for j in (0, 1):
            for k in (0, 1):
                for src in (0, 1):
                    perm.append((j * 4 + k * 2 + src, k * 4 + j * 2 + target_layer(k)))
        return [
            lax.ppermute(value, ("yl", "core", "layer"), [p for p in perm if p[0] % 2 == src])
            for src in (0, 1)
        ]

    got = route(part_own, lambda k: k) + route(part_other, lambda k: 1 - k)
    total = (got[0] + got[1]) + (got[2] + got[3])
    return total * kept


def solution(mesh):
    rows, cols, layers = mesh.devices.shape
    fine = Mesh(mesh.devices.reshape(rows // 4, 2, 2, cols // 2, 2, layers), AXES)
    return jax.shard_map(
        lambda *args: shards(*args, cols),
        mesh=fine,
        in_specs=(
            P("layer", ROW, COL),
            P("layer", ROW, COL),
            P("layer", ROW, COL),
            P("layer", None, COL),
            P(ROW, COL),
        ),
        out_specs=P(ROW, ("x", "core", "layer")),
        check_vma=False,
    )
```

```python
import jax
import jax.numpy as jnp
from jax import lax
from jax.sharding import PartitionSpec as P

BLOCK = 64


def expand(block_mask):
    widened = jnp.repeat(block_mask.astype(jnp.float32), BLOCK, axis=-2)
    return jnp.repeat(widened, BLOCK, axis=-1)


def gather_cols(block, axis_name, n):
    parts = [block]
    for shift in range(1, n):
        parts.append(lax.ppermute(block, axis_name, [((i + shift) % n, i) for i in range(n)]))
    twice = jnp.concatenate(parts + parts, axis=1)
    start = (n - lax.axis_index(axis_name)) * block.shape[1]
    return lax.dynamic_slice_in_dim(twice, start, n * block.shape[1], axis=1)


def product_dot(a, b):
    return jnp.dot(a, b, precision=lax.Precision.HIGH, preferred_element_type=jnp.float32)


def shards(density, dens_mask, hamiltonian, ham_mask, filter_mask, n_col):
    layer = lax.axis_index("layer")
    dens_vals = (density * expand(dens_mask))[0]
    ham_count = hamiltonian.shape[1]
    picked = lax.dynamic_slice_in_dim(
        ham_mask[0], lax.axis_index("row") * (ham_count // BLOCK), ham_count // BLOCK, axis=0
    )
    ham_vals = hamiltonian[0] * expand(picked)
    half = ham_vals.shape[1] // 2
    kept = lax.dynamic_slice_in_dim(expand(filter_mask), layer * half, half, axis=1)

    send_half = lax.dynamic_slice_in_dim(ham_vals, (1 - layer) * half, half, axis=1)
    keep_half = lax.dynamic_slice_in_dim(ham_vals, layer * half, half, axis=1)
    ham_panel = lax.all_gather(jnp.concatenate([send_half, keep_half], axis=1), "row", axis=0, tiled=True)
    dens_row = gather_cols(dens_vals, "col", n_col)
    received = lax.ppermute(product_dot(dens_row, ham_panel[:, :half]), "layer", [(0, 1), (1, 0)])
    own = lax.optimization_barrier(product_dot(dens_row, ham_panel[:, half:]))
    return (own + received) * kept


def solution(mesh):
    n_col = mesh.shape["col"]
    return jax.shard_map(
        lambda *args: shards(*args, n_col),
        mesh=mesh,
        in_specs=(
            P("layer", "row", "col"),
            P("layer", "row", "col"),
            P("layer", "row", "col"),
            P("layer", None, "col"),
            P("row", "col"),
        ),
        out_specs=P("row", ("col", "layer")),
        check_vma=False,
    )
```

```python
import jax
import jax.numpy as jnp
from jax import lax
from jax.sharding import PartitionSpec as P

BLOCK = 64


def expand(block_mask):
    widened = jnp.repeat(block_mask.astype(jnp.float32), BLOCK, axis=-2)
    return jnp.repeat(widened, BLOCK, axis=-1)


def gather_cols(block, axis_name, n):
    parts = [block]
    for shift in range(1, n):
        parts.append(lax.ppermute(block, axis_name, [((i + shift) % n, i) for i in range(n)]))
    twice = jnp.concatenate(parts + parts, axis=1)
    start = (n - lax.axis_index(axis_name)) * block.shape[1]
    return lax.dynamic_slice_in_dim(twice, start, n * block.shape[1], axis=1)


def product_dot(a, b):
    return jnp.dot(a, b, precision=lax.Precision.HIGH, preferred_element_type=jnp.float32)


def shards(density, dens_mask, hamiltonian, ham_mask, filter_mask, n_col):
    layer = lax.axis_index("layer")
    dens_vals = (density * expand(dens_mask))[0]
    ham_count = hamiltonian.shape[1]
    picked = lax.dynamic_slice_in_dim(
        ham_mask[0], lax.axis_index("row") * (ham_count // BLOCK), ham_count // BLOCK, axis=0
    )
    ham_vals = hamiltonian[0] * expand(picked)
    half = ham_vals.shape[1] // 2
    kept = lax.dynamic_slice_in_dim(expand(filter_mask), layer * half, half, axis=1)

    send_half = lax.dynamic_slice_in_dim(ham_vals, (1 - layer) * half, half, axis=1)
    keep_half = lax.dynamic_slice_in_dim(ham_vals, layer * half, half, axis=1)
    ham_panel = lax.all_gather(jnp.concatenate([send_half, keep_half], axis=1), "row", axis=0, tiled=True)
    dens_row = gather_cols(dens_vals, "col", n_col)
    step = half // 2
    received = jnp.concatenate(
        [
            lax.ppermute(product_dot(dens_row, ham_panel[:, i:i + step]), "layer", [(0, 1), (1, 0)])
            for i in range(0, half, step)
        ],
        axis=1,
    )
    own = lax.optimization_barrier(product_dot(dens_row, ham_panel[:, half:]))
    return (own + received) * kept


def solution(mesh):
    n_col = mesh.shape["col"]
    return jax.shard_map(
        lambda *args: shards(*args, n_col),
        mesh=mesh,
        in_specs=(
            P("layer", "row", "col"),
            P("layer", "row", "col"),
            P("layer", "row", "col"),
            P("layer", None, "col"),
            P("row", "col"),
        ),
        out_specs=P("row", ("col", "layer")),
        check_vma=False,
    )
```

```python
import jax
import jax.numpy as jnp
from jax import lax
from jax.sharding import PartitionSpec as P

BLOCK = 64


def expand(block_mask):
    widened = jnp.repeat(block_mask.astype(jnp.float32), BLOCK, axis=-2)
    return jnp.repeat(widened, BLOCK, axis=-1)


def gather_cols(block, axis_name, n):
    index = lax.axis_index(axis_name)
    width = block.shape[1]
    full = jnp.zeros((block.shape[0], n * width), block.dtype)
    for shift in range(n):
        part = block if shift == 0 else lax.ppermute(block, axis_name, [((i + shift) % n, i) for i in range(n)])
        full = lax.dynamic_update_slice_in_dim(full, part, ((index + shift) % n) * width, axis=1)
    return full


def product_dot(a, b):
    return jnp.dot(a, b, precision=lax.Precision.HIGH, preferred_element_type=jnp.float32)


def shards(density, dens_mask, hamiltonian, ham_mask, filter_mask, n_col):
    layer = lax.axis_index("layer")
    dens_vals = (density * expand(dens_mask))[0]
    ham_count = hamiltonian.shape[1]
    picked = lax.dynamic_slice_in_dim(
        ham_mask[0], lax.axis_index("row") * (ham_count // BLOCK), ham_count // BLOCK, axis=0
    )
    ham_vals = hamiltonian[0] * expand(picked)
    half = ham_vals.shape[1] // 2
    kept = lax.dynamic_slice_in_dim(expand(filter_mask), layer * half, half, axis=1)

    send_half = lax.dynamic_slice_in_dim(ham_vals, (1 - layer) * half, half, axis=1)
    keep_half = lax.dynamic_slice_in_dim(ham_vals, layer * half, half, axis=1)
    ham_panel = lax.all_gather(jnp.concatenate([send_half, keep_half], axis=1), "row", axis=0, tiled=True)
    dens_row = gather_cols(dens_vals, "col", n_col)
    step = half // 4
    received = jnp.concatenate(
        [
            lax.ppermute(product_dot(dens_row, ham_panel[:, i:i + step]), "layer", [(0, 1), (1, 0)])
            for i in range(0, half, step)
        ],
        axis=1,
    )
    own = lax.optimization_barrier(product_dot(dens_row, ham_panel[:, half:]))
    return (own + received) * kept


def solution(mesh):
    n_col = mesh.shape["col"]
    return jax.shard_map(
        lambda *args: shards(*args, n_col),
        mesh=mesh,
        in_specs=(
            P("layer", "row", "col"),
            P("layer", "row", "col"),
            P("layer", "row", "col"),
            P("layer", None, "col"),
            P("row", "col"),
        ),
        out_specs=P("row", ("col", "layer")),
        check_vma=False,
    )
```

```python
import jax
import jax.numpy as jnp
from jax import lax
from jax.sharding import PartitionSpec as P

BLOCK = 64


def expand(block_mask):
    widened = jnp.repeat(block_mask.astype(jnp.float32), BLOCK, axis=-2)
    return jnp.repeat(widened, BLOCK, axis=-1)


def gather_cols(block, axis_name, n):
    index = lax.axis_index(axis_name)
    width = block.shape[1]
    full = jnp.zeros((block.shape[0], n * width), block.dtype)
    for shift in range(n):
        part = block if shift == 0 else lax.ppermute(block, axis_name, [((i + shift) % n, i) for i in range(n)])
        full = lax.dynamic_update_slice_in_dim(full, part, ((index + shift) % n) * width, axis=1)
    return full


def product_dot(a, b):
    return jnp.dot(a, b, precision=lax.Precision.HIGH, preferred_element_type=jnp.float32)


def shards(density, dens_mask, hamiltonian, ham_mask, filter_mask, n_col):
    layer = lax.axis_index("layer")
    dens_vals = (density * expand(dens_mask))[0]
    ham_count = hamiltonian.shape[1]
    picked = lax.dynamic_slice_in_dim(
        ham_mask[0], lax.axis_index("row") * (ham_count // BLOCK), ham_count // BLOCK, axis=0
    )
    ham_vals = hamiltonian[0] * expand(picked)
    half = ham_vals.shape[1] // 2
    kept = lax.dynamic_slice_in_dim(expand(filter_mask), layer * half, half, axis=1)

    ham_panel = lax.all_gather(ham_vals, "row", axis=0, tiled=True)
    dens_row = gather_cols(dens_vals, "col", n_col)
    step = half // 4
    send_start = (1 - layer) * half
    received = jnp.concatenate(
        [
            lax.ppermute(
                product_dot(dens_row, lax.dynamic_slice_in_dim(ham_panel, send_start + i, step, axis=1)),
                "layer",
                [(0, 1), (1, 0)],
            )
            for i in range(0, half, step)
        ],
        axis=1,
    )
    own = lax.optimization_barrier(
        product_dot(dens_row, lax.dynamic_slice_in_dim(ham_panel, layer * half, half, axis=1))
    )
    return (own + received) * kept


def solution(mesh):
    n_col = mesh.shape["col"]
    return jax.shard_map(
        lambda *args: shards(*args, n_col),
        mesh=mesh,
        in_specs=(
            P("layer", "row", "col"),
            P("layer", "row", "col"),
            P("layer", "row", "col"),
            P("layer", None, "col"),
            P("row", "col"),
        ),
        out_specs=P("row", ("col", "layer")),
        check_vma=False,
    )
```

```python
import jax
import jax.numpy as jnp
from jax import lax
from jax.sharding import PartitionSpec as P

BLOCK = 64


def expand(block_mask):
    widened = jnp.repeat(block_mask.astype(jnp.float32), BLOCK, axis=-2)
    return jnp.repeat(widened, BLOCK, axis=-1)


def gather_cols(block, axis_name, n):
    index = lax.axis_index(axis_name)
    width = block.shape[1]
    full = jnp.zeros((block.shape[0], n * width), block.dtype)
    for shift in range(n):
        part = block if shift == 0 else lax.ppermute(block, axis_name, [((i + shift) % n, i) for i in range(n)])
        full = lax.dynamic_update_slice_in_dim(full, part, ((index + shift) % n) * width, axis=1)
    return full


def product_dot(a, b):
    return jnp.dot(a, b, precision=lax.Precision.HIGH, preferred_element_type=jnp.float32)


def shards(density, dens_mask, hamiltonian, ham_mask, filter_mask, n_col):
    layer = lax.axis_index("layer")
    dens_vals = (density * expand(dens_mask))[0]
    ham_count = hamiltonian.shape[1]
    picked = lax.dynamic_slice_in_dim(
        ham_mask[0], lax.axis_index("row") * (ham_count // BLOCK), ham_count // BLOCK, axis=0
    )
    ham_vals = hamiltonian[0] * expand(picked)
    half = ham_vals.shape[1] // 2
    kept = lax.dynamic_slice_in_dim(expand(filter_mask), layer * half, half, axis=1)

    send_half = lax.dynamic_slice_in_dim(ham_vals, (1 - layer) * half, half, axis=1)
    keep_half = lax.dynamic_slice_in_dim(ham_vals, layer * half, half, axis=1)
    ham_panel = lax.all_gather(jnp.concatenate([send_half, keep_half], axis=1), "row", axis=0, tiled=True)
    dens_row = gather_cols(dens_vals, "col", n_col)
    bounds = [0, half // 4, half // 2, half]
    received = jnp.concatenate(
        [
            lax.ppermute(product_dot(dens_row, ham_panel[:, a:b]), "layer", [(0, 1), (1, 0)])
            for a, b in zip(bounds[:-1], bounds[1:])
        ],
        axis=1,
    )
    own = lax.optimization_barrier(product_dot(dens_row, ham_panel[:, half:]))
    return (own + received) * kept


def solution(mesh):
    n_col = mesh.shape["col"]
    return jax.shard_map(
        lambda *args: shards(*args, n_col),
        mesh=mesh,
        in_specs=(
            P("layer", "row", "col"),
            P("layer", "row", "col"),
            P("layer", "row", "col"),
            P("layer", None, "col"),
            P("row", "col"),
        ),
        out_specs=P("row", ("col", "layer")),
        check_vma=False,
    )
```

```python
import jax
import jax.numpy as jnp
from jax import lax
from jax.sharding import PartitionSpec as P

BLOCK = 64


def expand(block_mask):
    widened = jnp.repeat(block_mask.astype(jnp.float32), BLOCK, axis=-2)
    return jnp.repeat(widened, BLOCK, axis=-1)


def gather_cols(block, axis_name, n):
    index = lax.axis_index(axis_name)
    width = block.shape[1]
    full = jnp.zeros((block.shape[0], n * width), block.dtype)
    for shift in range(n):
        part = block if shift == 0 else lax.ppermute(block, axis_name, [((i + shift) % n, i) for i in range(n)])
        full = lax.dynamic_update_slice_in_dim(full, part, ((index + shift) % n) * width, axis=1)
    return full


def product_dot(a, b):
    return jnp.dot(a, b, precision=lax.Precision.HIGH, preferred_element_type=jnp.float32)


def split_bf16(x):
    high = lax.reduce_precision(x, exponent_bits=8, mantissa_bits=7)
    return high.astype(jnp.bfloat16), (x - high).astype(jnp.bfloat16)


def split_dot(a_parts, b):
    b_parts = split_bf16(b)
    one = lambda p, q: jnp.dot(p, q, preferred_element_type=jnp.float32)
    return one(a_parts[0], b_parts[0]) + (one(a_parts[0], b_parts[1]) + one(a_parts[1], b_parts[0]))


def shards(density, dens_mask, hamiltonian, ham_mask, filter_mask, n_col):
    layer = lax.axis_index("layer")
    dens_vals = (density * expand(dens_mask))[0]
    ham_count = hamiltonian.shape[1]
    picked = lax.dynamic_slice_in_dim(
        ham_mask[0], lax.axis_index("row") * (ham_count // BLOCK), ham_count // BLOCK, axis=0
    )
    ham_vals = hamiltonian[0] * expand(picked)
    half = ham_vals.shape[1] // 2
    kept = lax.dynamic_slice_in_dim(expand(filter_mask), layer * half, half, axis=1)

    send_half = lax.dynamic_slice_in_dim(ham_vals, (1 - layer) * half, half, axis=1)
    keep_half = lax.dynamic_slice_in_dim(ham_vals, layer * half, half, axis=1)
    ham_panel = lax.all_gather(jnp.concatenate([send_half, keep_half], axis=1), "row", axis=0, tiled=True)
    dens_row = gather_cols(dens_vals, "col", n_col)
    step = half // 4
    dens_parts = split_bf16(dens_row)
    received = jnp.concatenate(
        [
            lax.ppermute(
                (split_dot(dens_parts, ham_panel[:, i:i + step]) if i == 0 else product_dot(dens_row, ham_panel[:, i:i + step])),
                "layer",
                [(0, 1), (1, 0)],
            )
            for i in range(0, half, step)
        ],
        axis=1,
    )
    own = lax.optimization_barrier(product_dot(dens_row, ham_panel[:, half:]))
    return (own + received) * kept


def solution(mesh):
    n_col = mesh.shape["col"]
    return jax.shard_map(
        lambda *args: shards(*args, n_col),
        mesh=mesh,
        in_specs=(
            P("layer", "row", "col"),
            P("layer", "row", "col"),
            P("layer", "row", "col"),
            P("layer", None, "col"),
            P("row", "col"),
        ),
        out_specs=P("row", ("col", "layer")),
        check_vma=False,
    )
```
